256 devices in a mesh: seq: 32 (over y, x, core), ch: 8 (over z).
Axes of the slice: x: 4, y: 4, z: 8, core: 2. Of those that a mesh axis runs over, the one named last changes fastest.
Arguments:
- inputs: bfloat16 [8192, 4096], P('seq', 'ch'), may hold values from -6 to 6
- w_value: bfloat16 [4096, 4096], P(None, 'ch'), may hold values from -0.09375 to 0.09375
- gates: bfloat16 [2, 8192, 4096], P(None, 'seq', 'ch'), may hold values from -6 to 6
- decay_rate: float32 [16, 4096], P(None, 'ch'), may hold values from 0 to 0.125, as said below
- residue: float32 [16, 4096], P(None, 'ch'), may hold values from -5 to 5
- fir_taps: float32 [128, 4096], P(None, 'ch'), may hold values from -0.5 to 0.5
- skip_gain: float32 [4096], P('ch'), may hold values from -4 to 4
Outputs:
- mixed: bfloat16 [8192, 4096], P('seq', 'ch')
The draws below stay inside these ranges and needn't reach their ends.
Inputs may be any that keep to these rules, and one draw needn't show every extreme that they name: `decay_rate`: every rate is positive.
All inputs are finite; a program needn't handle non-finite values.
Results may differ from the reference program's by a relative error of at most 0.0049.
Values may be sent and summed in bfloat16 or wider, within the bound.
No kernel may reach another device: no remote copies, remote signals or barrier semaphores. Data moves between devices by JAX's collectives and lax.ppermute only.
A program may use at most 320 MiB of HBM per device.

```python
import jax
import jax.numpy as jnp
from jax import lax

D = 4096
POLES = 16
TAPS = 128
TOKENS = 8192


def draw_decay_rate(key, part):
    first, second, third = jax.random.split(key, 3)
    slow_share = 0.5
    picker = jax.random.uniform(first, (POLES, D), jnp.float32)
    slow_rate = jnp.exp(jnp.log(0.05 / TOKENS) + jax.random.uniform(second, (POLES, D), jnp.float32) * jnp.log(30.0))
    fast_rate = jnp.exp(jnp.log(1.0 / 64.0) + jax.random.uniform(third, (POLES, D), jnp.float32) * jnp.log(8.0))
    return jnp.where(picker < slow_share, slow_rate, fast_rate).astype(jnp.float32)


def block_levels(own_key, extent, cuts, least, high):
    loudness, own = 1.0, jax.random.fold_in(own_key, 6)
    for position, shards_of in cuts:
        steps = jnp.exp(jax.random.uniform(jax.random.fold_in(own, position), (shards_of,), jnp.float32, least / len(cuts), high / len(cuts)))
        loudness = loudness * jnp.repeat(steps, extent[position] // shards_of).reshape([-1 if axis == position else 1 for axis in range(len(extent))])
    return loudness


def scatter_about(stream_key, dims, spread, bound, shards=(), held_as=jnp.bfloat16):
    array = jax.random.normal(stream_key, dims, jnp.float32) * spread
    if len(shards) > 0:
        array = block_levels(stream_key, dims, shards, -0.22, 0.18) * array
    return jnp.clip(array, min=-bound, max=bound).astype(held_as)


def setup_inputs(seed: int = 0) -> dict:
    keys = jax.random.split(jax.random.key(seed), 8)
    inputs = scatter_about(keys[0], (TOKENS, D), 1.0, 6.0, ((0, 32), (1, 8)))
    w_value = scatter_about(keys[1], (D, D), D ** -0.5, 0.09375, ((1, 8),))
    gates = scatter_about(keys[2], (2, TOKENS, D), 1.0, 6.0, ((1, 32), (2, 8)))
    decay_rate = draw_decay_rate(jax.random.fold_in(keys[7], 71), 0)
    residue = scatter_about(keys[4], (POLES, D), 1.0, 5.0, ((1, 8),), jnp.float32)
    fir_taps = scatter_about(keys[5], (TAPS, D), TAPS ** -0.5, 0.5, ((1, 8),), jnp.float32)
    skip_gain = scatter_about(keys[6], (D,), 1.0, 4.0, ((0, 8),), jnp.float32)
    return {"inputs": inputs, "w_value": w_value, "gates": gates, "decay_rate": decay_rate, "residue": residue, "fir_taps": fir_taps, "skip_gain": skip_gain}


def reference(inputs, w_value, gates, decay_rate, residue, fir_taps, skip_gain):
    projected = jnp.dot(inputs, w_value, preferred_element_type=jnp.float32)
    signal_low = (gates[1].astype(jnp.float32) * projected).astype(jnp.bfloat16)
    signal = lax.optimization_barrier(signal_low).astype(jnp.float32)
    modal_coef = residue * jnp.sqrt(-jnp.expm1(-2.0 * decay_rate))
    chan_block_size = min(256, D)
    fft_length = 2 * TOKENS

    def convolve_block(block_index):
        start = block_index * chan_block_size
        chan_block = lax.dynamic_slice_in_dim(signal, start, chan_block_size, 1)
        rates = lax.dynamic_slice_in_dim(decay_rate, start, chan_block_size, 1)
        coefs = lax.dynamic_slice_in_dim(modal_coef, start, chan_block_size, 1)
        heads = lax.dynamic_slice_in_dim(fir_taps, start, chan_block_size, 1)
        lag_times = jnp.arange(TOKENS).astype(signal.dtype)[:, None]
        filter_taps = jnp.zeros((TOKENS, chan_block_size), signal.dtype)
        for pole in range(POLES):
            filter_taps = filter_taps + coefs[pole] * jnp.exp(-rates[pole] * lag_times)
        filter_taps = filter_taps.at[:TAPS].add(heads)
        spectrum = jnp.fft.rfft(chan_block, n=fft_length, axis=0) * jnp.fft.rfft(filter_taps, n=fft_length, axis=0)
        return jnp.fft.irfft(spectrum, n=fft_length, axis=0)[:TOKENS].astype(signal.dtype)
    conv_blocks = lax.map(convolve_block, jnp.arange(D // chan_block_size).astype(jnp.int32))
    conv = jnp.transpose(conv_blocks, (1, 0, 2)).reshape(TOKENS, D)
    mixed = gates[0].astype(jnp.float32) * (conv + skip_gain * signal)
    return mixed.astype(jnp.bfloat16)
```

```python
import functools

import jax
import jax.numpy as jnp
from jax import lax
from jax.experimental import pallas as pl
from jax.experimental.pallas import tpu as pltpu
from jax.sharding import PartitionSpec as P


LANES = 128
SUB = 8
CHUNK = 64


def from_behind(shard, axis, by):
    devices = lax.axis_size(axis)
    pairs = [(i, i + by) for i in range(devices) if 0 <= i + by < devices]
    return lax.ppermute(shard, axis, pairs)


def conv_kernel(x_ref, tail_ref, h_ref, fir_ref, out_ref, xz, xs, xtz, xts):
    rows = x_ref.shape[0]
    taps = fir_ref.shape[0]
    xz[pl.ds(0, rows), :] = jnp.zeros((rows, LANES), jnp.float32)
    xz[pl.ds(rows, rows), :] = x_ref[...]
    xz[pl.ds(2 * rows, SUB), :] = jnp.zeros((SUB, LANES), jnp.float32)
    xtz[pl.ds(0, taps), :] = tail_ref[...]
    xtz[pl.ds(taps, taps + SUB), :] = jnp.zeros((taps + SUB, LANES), jnp.float32)
    for b in range(SUB):
        xs[b] = xz[pl.ds(SUB - b, 2 * rows), :]
        xts[b] = xtz[pl.ds(SUB - b, 2 * taps), :]

    for q in range(rows // CHUNK):
        t0 = q * CHUNK

        def body_a(a, acc, t0=t0):
            start = pl.multiple_of(t0 + rows - SUB - SUB * a, SUB)
            for b in range(SUB):
                hrow = h_ref[pl.ds(SUB * a + b, 1), :]
                acc = acc + hrow * xs[b, pl.ds(start, CHUNK), :]
            return acc

        acc = jnp.zeros((CHUNK, LANES), jnp.float32)
        acc = lax.fori_loop(0, (t0 + CHUNK) // SUB, body_a, acc)
        if t0 < taps:

            def body_b(a, acc, t0=t0):
                start = pl.multiple_of(t0 + taps - SUB - SUB * a, SUB)
                for b in range(SUB):
                    frow = fir_ref[pl.ds(SUB * a + b, 1), :]
                    acc = acc + frow * xts[b, pl.ds(start, CHUNK), :]
                return acc

            acc = lax.fori_loop(t0 // SUB, taps // SUB, body_b, acc)
        out_ref[pl.ds(t0, CHUNK), :] = acc


def local_conv(x, tail, h, fir):
    rows, width = x.shape
    taps = fir.shape[0]
    blocks = width // LANES
    return pl.pallas_call(
        conv_kernel,
        grid=(blocks,),
        in_specs=[
            pl.BlockSpec((rows, LANES), lambda j: (0, j)),
            pl.BlockSpec((taps, LANES), lambda j: (0, j)),
            pl.BlockSpec((rows, LANES), lambda j: (0, j)),
            pl.BlockSpec((taps, LANES), lambda j: (0, j)),
        ],
        out_specs=pl.BlockSpec((rows, LANES), lambda j: (0, j)),
        out_shape=jax.ShapeDtypeStruct((rows, width), jnp.float32),
        scratch_shapes=[
            pltpu.VMEM((2 * rows + SUB, LANES), jnp.float32),
            pltpu.VMEM((SUB, 2 * rows, LANES), jnp.float32),
            pltpu.VMEM((2 * taps + SUB, LANES), jnp.float32),
            pltpu.VMEM((SUB, 2 * taps, LANES), jnp.float32),
        ],
        cost_estimate=pl.CostEstimate(
            flops=2 * rows * (rows // 2 + taps // 2) * width,
            bytes_accessed=4 * width * (3 * rows + 2 * taps),
            transcendentals=0,
        ),
    )(x, tail, h, fir)


def on_device(inputs, w_value, gates, decay_rate, residue, fir_taps, skip_gain):
    rows = inputs.shape[0]
    taps = fir_taps.shape[0]
    sections = lax.axis_size("seq")
    me = lax.axis_index("seq")

    projected = jnp.dot(
        lax.all_gather(inputs, "ch", axis=1, tiled=True),
        w_value,
        preferred_element_type=jnp.float32,
    )
    gated_value = (gates[1].astype(jnp.float32) * projected).astype(jnp.bfloat16)
    x = gated_value.astype(jnp.float32)

    modal_coef = residue * jnp.sqrt(-jnp.expm1(-2.0 * decay_rate))
    lags = jnp.arange(rows, dtype=jnp.float32)

    back = jnp.exp(-decay_rate[:, None, :] * (rows - 1 - lags)[None, :, None])
    local_state = jnp.sum(back * x[None], axis=1)
    all_states = lax.all_gather(local_state, "seq", axis=0, tiled=False)

    tail = from_behind(gated_value[rows - taps :], "seq", 1).astype(jnp.float32)

    h = jnp.sum(
        modal_coef[:, None, :] * jnp.exp(-decay_rate[:, None, :] * lags[None, :, None]),
        axis=0,
    )
    h = h.at[:taps].add(fir_taps)
    conv = local_conv(x, tail, h, fir_taps)

    src = jnp.arange(sections)
    hops = (me - 1 - src).astype(jnp.float32)
    weight = jnp.where(
        (src < me)[:, None, None],
        jnp.exp(-decay_rate[None] * (rows * jnp.maximum(hops, 0.0))[:, None, None]),
        0.0,
    )
    incoming = jnp.sum(weight * all_states, axis=0)
    carried = modal_coef * incoming
    corr = jnp.sum(
        carried[:, None, :] * jnp.exp(-decay_rate[:, None, :] * (lags + 1.0)[None, :, None]),
        axis=0,
    )
    mixed = gates[0].astype(jnp.float32) * (conv + corr + skip_gain * x)
    return mixed.astype(jnp.bfloat16)


def solution(mesh):
    in_specs = (
        P("seq", "ch"),
        P(None, "ch"),
        P(None, "seq", "ch"),
        P(None, "ch"),
        P(None, "ch"),
        P(None, "ch"),
        P("ch"),
    )
    out_specs = P("seq", "ch")
    return jax.shard_map(
        on_device, mesh=mesh, in_specs=in_specs, out_specs=out_specs, check_vma=False
    )
```

```python
import functools

import jax
import jax.numpy as jnp
from jax import lax
from jax.experimental import pallas as pl
from jax.experimental.pallas import tpu as pltpu
from jax.sharding import PartitionSpec as P


LANES = 128
SUB = 8
CHUNK = 64


def from_behind(shard, axis, by):
    devices = lax.axis_size(axis)
    pairs = [(i, i + by) for i in range(devices) if 0 <= i + by < devices]
    return lax.ppermute(shard, axis, pairs)


def conv_kernel(x_ref, tail_ref, h_ref, fir_ref, out_ref, xz, xs, xtz, xts):
    rows = x_ref.shape[0]
    taps = fir_ref.shape[0]
    xz[pl.ds(0, rows), :] = jnp.zeros((rows, LANES), jnp.float32)
    xz[pl.ds(rows, rows), :] = x_ref[...]
    xz[pl.ds(2 * rows, SUB), :] = jnp.zeros((SUB, LANES), jnp.float32)
    xtz[pl.ds(0, taps), :] = tail_ref[...]
    xtz[pl.ds(taps, taps + SUB), :] = jnp.zeros((taps + SUB, LANES), jnp.float32)
    for b in range(SUB):
        xs[b] = xz[pl.ds(SUB - b, 2 * rows), :]
        xts[b] = xtz[pl.ds(SUB - b, 2 * taps), :]

    for q in range(rows // CHUNK):
        t0 = q * CHUNK

        def body_a(a, acc, t0=t0):
            start = pl.multiple_of(t0 + rows - SUB - SUB * a, SUB)
            for b in range(SUB):
                hrow = h_ref[pl.ds(SUB * a + b, 1), :]
                acc = acc + hrow * xs[b, pl.ds(start, CHUNK), :]
            return acc

        acc = jnp.zeros((CHUNK, LANES), jnp.float32)
        acc = lax.fori_loop(0, (t0 + CHUNK) // SUB, body_a, acc)
        if t0 < taps:

            def body_b(a, acc, t0=t0):
                start = pl.multiple_of(t0 + taps - SUB - SUB * a, SUB)
                for b in range(SUB):
                    frow = fir_ref[pl.ds(SUB * a + b, 1), :]
                    acc = acc + frow * xts[b, pl.ds(start, CHUNK), :]
                return acc

            acc = lax.fori_loop(t0 // SUB, taps // SUB, body_b, acc)
        out_ref[pl.ds(t0, CHUNK), :] = acc


def local_conv(x, tail, h, fir):
    rows, width = x.shape
    taps = fir.shape[0]
    blocks = width // LANES
    return pl.pallas_call(
        conv_kernel,
        grid=(blocks,),
        in_specs=[
            pl.BlockSpec((rows, LANES), lambda j: (0, j)),
            pl.BlockSpec((taps, LANES), lambda j: (0, j)),
            pl.BlockSpec((rows, LANES), lambda j: (0, j)),
            pl.BlockSpec((taps, LANES), lambda j: (0, j)),
        ],
        out_specs=pl.BlockSpec((rows, LANES), lambda j: (0, j)),
        out_shape=jax.ShapeDtypeStruct((rows, width), jnp.float32),
        scratch_shapes=[
            pltpu.VMEM((2 * rows + SUB, LANES), jnp.float32),
            pltpu.VMEM((SUB, 2 * rows, LANES), jnp.float32),
            pltpu.VMEM((2 * taps + SUB, LANES), jnp.float32),
            pltpu.VMEM((SUB, 2 * taps, LANES), jnp.float32),
        ],
        cost_estimate=pl.CostEstimate(
            flops=2 * rows * (rows // 2 + taps // 2) * width,
            bytes_accessed=4 * width * (3 * rows + 2 * taps),
            transcendentals=0,
        ),
    )(x, tail, h, fir)


def prefix_state(local_state, decay_rate, rows, sections):
    def power(k):
        return jnp.exp(-decay_rate * float(rows * k))

    acc = jnp.zeros_like(local_state)
    for k in range(1, 5):
        if k < sections:
            acc = acc + power(k - 1) * from_behind(local_state, "seq", k)
    window = 4
    while window < sections:
        step = acc
        for m in range(1, 4):
            shift = window * m
            if shift < sections:
                acc = acc + power(shift) * from_behind(step, "seq", shift)
        window *= 4
    return acc


def on_device(inputs, w_value, gates, decay_rate, residue, fir_taps, skip_gain):
    rows = inputs.shape[0]
    taps = fir_taps.shape[0]
    sections = lax.axis_size("seq")
    me = lax.axis_index("seq")

    projected = jnp.dot(
        lax.all_gather(inputs, "ch", axis=1, tiled=True),
        w_value,
        preferred_element_type=jnp.float32,
    )
    gated_value = (gates[1].astype(jnp.float32) * projected).astype(jnp.bfloat16)
    x = gated_value.astype(jnp.float32)

    modal_coef = residue * jnp.sqrt(-jnp.expm1(-2.0 * decay_rate))
    lags = jnp.arange(rows, dtype=jnp.float32)

    back = jnp.exp(-decay_rate[:, None, :] * (rows - 1 - lags)[None, :, None])
    local_state = jnp.sum(back * x[None], axis=1)
    incoming = prefix_state(local_state, decay_rate, rows, sections)

    tail = from_behind(gated_value[rows - taps :], "seq", 1).astype(jnp.float32)

    h = jnp.sum(
        modal_coef[:, None, :] * jnp.exp(-decay_rate[:, None, :] * lags[None, :, None]),
        axis=0,
    )
    h = h.at[:taps].add(fir_taps)
    conv = local_conv(x, tail, h, fir_taps)

    carried = modal_coef * incoming
    corr = jnp.sum(
        carried[:, None, :] * jnp.exp(-decay_rate[:, None, :] * (lags + 1.0)[None, :, None]),
        axis=0,
    )
    mixed = gates[0].astype(jnp.float32) * (conv + corr + skip_gain * x)
    return mixed.astype(jnp.bfloat16)


def solution(mesh):
    in_specs = (
        P("seq", "ch"),
        P(None, "ch"),
        P(None, "seq", "ch"),
        P(None, "ch"),
        P(None, "ch"),
        P(None, "ch"),
        P("ch"),
    )
    out_specs = P("seq", "ch")
    return jax.shard_map(
        on_device, mesh=mesh, in_specs=in_specs, out_specs=out_specs, check_vma=False
    )
```
